768 devices in a mesh: row: 24 (over z, y_hi), col: 32 (over x, y_lo, core).
Axes of the slice: x: 4, y: 8 (y_hi: 2, y_lo: 4; y = y_hi * 4 + y_lo), z: 12, core: 2. Of those that a mesh axis runs over, the one named last changes fastest.
Arguments:
- iterate: bfloat16 [7680, 7680], P('row', 'col'), may hold values from -2 to 2
- pattern: int32 [120, 120], replicated, may hold values 0 or 1
Outputs:
- squared: bfloat16 [7680, 7680], P('row', 'col')
- traces: float32 [2], replicated
The draws below stay inside these ranges and needn't reach their ends.
All inputs are finite; a program needn't handle non-finite values.
Results may differ from the reference program's by a relative error of at most 0.001.
Values may be sent and summed in bfloat16 or wider, within the bound.
No kernel may reach another device: no remote copies, remote signals or barrier semaphores. Data moves between devices by JAX's collectives and lax.ppermute only.
A program may use at most 64 MiB of HBM per device.

```python
import math
import jax
import jax.numpy as jnp

BS = 64
NB = 120


def draw_iterate(key, part):
    order_total = NB * BS
    key_base, key_rows, key_cols, key_diag = jax.random.split(key, 4)
    amplitude = (order_total * 0.25) ** (-0.25)
    row_scale = jnp.exp(jax.random.uniform(key_rows, (order_total, 1), minval=0.0, maxval=math.log(3.0)))
    col_scale = jnp.exp(jax.random.uniform(key_cols, (1, order_total), minval=0.0, maxval=math.log(3.0)))
    base_values = jax.random.truncated_normal(key_base, -4.0, 4.0, (order_total, order_total))
    off_values = jnp.clip(base_values * amplitude * row_scale * col_scale, -2.0, 2.0)
    position = jnp.arange(order_total, dtype=jnp.float32)
    diag_values = jax.random.uniform(key_diag, (order_total,), minval=0.15, maxval=0.5) * (1.0 + 2.0 * position / (order_total - 1))
    on_diagonal = jnp.arange(order_total)[:, None] == jnp.arange(order_total)[None, :]
    return jnp.where(on_diagonal, diag_values[None, :], off_values).astype(jnp.bfloat16)


def touch_ends(drawn, stream_key, smallest, top_value):
    index_at = [jax.random.randint(jax.random.fold_in(stream_key, axis), (), 0, length) for axis, length in enumerate(drawn.shape)]
    longest = drawn.shape.index(max(drawn.shape))
    next_to = index_at[:longest] + [(index_at[longest] + 1) % drawn.shape[longest]] + index_at[longest + 1:]
    return drawn.at[tuple(index_at)].set(smallest).at[tuple(next_to)].set(top_value)


def setup_inputs(seed: int = 0) -> dict:
    keys = jax.random.split(jax.random.key(seed), 3)
    return {
        "iterate": draw_iterate(jax.random.fold_in(keys[2], 71), 0),
        "pattern": touch_ends((jax.random.randint(keys[1], (NB, NB), 0, 2) < 1).astype(jnp.int32), jax.random.fold_in(keys[1], 1), 0, 1),
    }


def expand_blocks(block_mask):
    return jnp.repeat(jnp.repeat(block_mask, BS, axis=0), BS, axis=1) > 0


def reference(iterate, pattern):
    identity = jnp.eye(NB, dtype=jnp.int32)
    block_mask = jnp.maximum(pattern, identity)
    keep_mask = expand_blocks(block_mask)
    masked = jnp.where(keep_mask, iterate, jnp.zeros((), iterate.dtype))
    product = jnp.dot(masked, masked, preferred_element_type=jnp.float32)
    squared = jnp.where(keep_mask, product, jnp.zeros((), product.dtype)).astype(jnp.bfloat16)
    trace_first = jnp.sum(jnp.diagonal(masked).astype(jnp.float32))
    trace_second = jnp.sum(jnp.diagonal(product))
    traces = jnp.stack([trace_first, trace_second]) / (NB * BS)
    return squared, traces
```

```python
import functools

import jax
import jax.numpy as jnp
from jax import lax
from jax.experimental import pallas as pl
from jax.experimental.pallas import tpu as pltpu
from jax.sharding import Mesh
from jax.sharding import PartitionSpec as P

BS = 64
ROW = ("row_0", "row_1")
COL = ("col_0", "col_1", "col_2")
ROW_COL = ("row_0", "row_1", "col_0", "col_1", "col_2")


def tile_keep(block_mask, global_rows, global_cols):
    row_blocks = global_rows // BS
    col_blocks = global_cols // BS
    window = jnp.take(jnp.take(block_mask, row_blocks, axis=0), col_blocks, axis=1)
    return window > 0


def panel_kernel(left_ref, right_ref, out_ref):
    pieces, _, depth = left_ref.shape

    def body(piece, total):
        rows = pl.ds(pl.multiple_of(piece * depth, depth), depth)
        return total + jnp.dot(
            left_ref[piece], right_ref[rows, :], preferred_element_type=jnp.float32
        )

    out_ref[...] = lax.fori_loop(
        0, pieces, body, jnp.zeros(out_ref.shape, jnp.float32)
    )


def panel_product(left, right):
    pieces, tile_rows, depth = left.shape
    tile_cols = right.shape[1]
    return pl.pallas_call(
        panel_kernel,
        out_shape=jax.ShapeDtypeStruct((tile_rows, tile_cols), jnp.float32),
        in_specs=[pl.BlockSpec(memory_space=pltpu.VMEM)] * 2,
        out_specs=pl.BlockSpec(memory_space=pltpu.VMEM),
        cost_estimate=pl.CostEstimate(
            flops=2 * pieces * tile_rows * depth * tile_cols,
            bytes_accessed=2 * (left.size + right.size) + 4 * tile_rows * tile_cols,
            transcendentals=0,
        ),
    )(left, right)


def on_device(iterate, pattern):
    tile_rows, tile_cols = iterate.shape
    nblocks = pattern.shape[0]
    order_total = nblocks * BS
    row_index = lax.axis_index(ROW)
    col_index = lax.axis_index(COL)
    identity = jnp.eye(nblocks, dtype=jnp.int32)
    block_mask = jnp.maximum(pattern, identity)
    global_rows = row_index * tile_rows + jnp.arange(tile_rows, dtype=jnp.int32)
    global_cols = col_index * tile_cols + jnp.arange(tile_cols, dtype=jnp.int32)
    keep_mask = tile_keep(block_mask, global_rows, global_cols)
    masked = jnp.where(keep_mask, iterate, jnp.zeros((), iterate.dtype))
    on_diagonal = global_rows[:, None] == global_cols[None, :]
    trace_first = jnp.sum(
        jnp.where(on_diagonal, masked, jnp.zeros((), masked.dtype)), dtype=jnp.float32
    )
    left_panel = lax.all_gather(masked, COL, axis=0, tiled=False)
    right_panel = lax.all_gather(masked, ROW, axis=0, tiled=True)
    running = panel_product(left_panel, right_panel)
    squared = jnp.where(keep_mask, running, jnp.zeros((), jnp.float32)).astype(jnp.bfloat16)
    trace_second = jnp.sum(jnp.where(on_diagonal, running, jnp.zeros((), jnp.float32)))
    summed = lax.psum(jnp.stack([trace_first, trace_second]), ROW_COL)
    traces = summed / order_total
    return (squared, traces)


def solution(mesh):
    torus = Mesh(
        mesh.devices.reshape(12, 2, 4, 4, 2), ("row_0", "row_1", "col_0", "col_1", "col_2")
    )
    placed = (P(ROW, COL), P())
    return jax.shard_map(
        on_device, mesh=torus, in_specs=placed, out_specs=(P(ROW, COL), P()), check_vma=False
    )
```

```python
import functools

import jax
import jax.numpy as jnp
from jax import lax
from jax.experimental import pallas as pl
from jax.experimental.pallas import tpu as pltpu
from jax.sharding import Mesh
from jax.sharding import PartitionSpec as P

BS = 64
ROW = ("row_0", "row_1")
COL = ("col_0", "col_1", "col_2")
ROW_COL = ("row_0", "row_1", "col_0", "col_1", "col_2")


def tile_keep(block_mask, global_rows, global_cols):
    row_blocks = global_rows // BS
    col_blocks = global_cols // BS
    window = jnp.take(jnp.take(block_mask, row_blocks, axis=0), col_blocks, axis=1)
    return window > 0


def panel_kernel(left_ref, right_ref, out_ref):
    pieces, _, depth = left_ref.shape
    out_ref[...] = jnp.dot(left_ref[0], right_ref[0:depth, :], preferred_element_type=jnp.float32)
    for piece in range(1, pieces):
        out_ref[...] += jnp.dot(
            left_ref[piece],
            right_ref[piece * depth:(piece + 1) * depth, :],
            preferred_element_type=jnp.float32,
        )


def panel_product(left, right):
    pieces, tile_rows, depth = left.shape
    tile_cols = right.shape[1]
    return pl.pallas_call(
        panel_kernel,
        out_shape=jax.ShapeDtypeStruct((tile_rows, tile_cols), jnp.float32),
        in_specs=[pl.BlockSpec(memory_space=pltpu.VMEM)] * 2,
        out_specs=pl.BlockSpec(memory_space=pltpu.VMEM),
        cost_estimate=pl.CostEstimate(
            flops=2 * pieces * tile_rows * depth * tile_cols,
            bytes_accessed=2 * (left.size + right.size) + 4 * tile_rows * tile_cols,
            transcendentals=0,
        ),
    )(left, right)


def column_slab(masked):
    depth = lax.psum(1, "row_0")
    half = lax.axis_index("row_1")
    other = lax.ppermute(masked, "row_1", [(0, 1), (1, 0)])
    pair = jnp.where(
        half == 0,
        jnp.concatenate([masked, other]),
        jnp.concatenate([other, masked]),
    )
    here = lax.axis_index("row_0")
    slab = jnp.zeros((depth,) + pair.shape, pair.dtype)
    slab = lax.dynamic_update_index_in_dim(slab, pair, here, 0)
    forward = [(i, (i + 1) % depth) for i in range(depth)]
    backward = [(i, (i - 1) % depth) for i in range(depth)]
    ahead = pair
    behind = pair
    for step in range(1, depth // 2 + 1):
        ahead = lax.ppermute(ahead, "row_0", forward)
        slab = lax.dynamic_update_index_in_dim(slab, ahead, (here - step) % depth, 0)
        if step < depth - depth // 2:
            behind = lax.ppermute(behind, "row_0", backward)
            slab = lax.dynamic_update_index_in_dim(slab, behind, (here + step) % depth, 0)
    return slab.reshape(depth * pair.shape[0], pair.shape[1])


def on_device(iterate, pattern):
    tile_rows, tile_cols = iterate.shape
    nblocks = pattern.shape[0]
    order_total = nblocks * BS
    row_index = lax.axis_index(ROW)
    col_index = lax.axis_index(COL)
    identity = jnp.eye(nblocks, dtype=jnp.int32)
    block_mask = jnp.maximum(pattern, identity)
    global_rows = row_index * tile_rows + jnp.arange(tile_rows, dtype=jnp.int32)
    global_cols = col_index * tile_cols + jnp.arange(tile_cols, dtype=jnp.int32)
    keep_mask = tile_keep(block_mask, global_rows, global_cols)
    masked = jnp.where(keep_mask, iterate, jnp.zeros((), iterate.dtype))
    on_diagonal = global_rows[:, None] == global_cols[None, :]
    trace_first = jnp.sum(
        jnp.where(on_diagonal, masked, jnp.zeros((), masked.dtype)), dtype=jnp.float32
    )
    left_panel = lax.all_gather(masked, COL, axis=0, tiled=False)
    right_panel = column_slab(masked)
    running = panel_product(left_panel, right_panel)
    squared = jnp.where(keep_mask, running, jnp.zeros((), jnp.float32)).astype(jnp.bfloat16)
    trace_second = jnp.sum(jnp.where(on_diagonal, running, jnp.zeros((), jnp.float32)))
    summed = jnp.stack([trace_first, trace_second])
    for axis in ROW_COL:
        summed = lax.psum(summed, axis)
    traces = summed / order_total
    return (squared, traces)


def solution(mesh):
    torus = Mesh(
        mesh.devices.reshape(12, 2, 4, 4, 2), ("row_0", "row_1", "col_0", "col_1", "col_2")
    )
    placed = (P(ROW, COL), P())
    return jax.shard_map(
        on_device, mesh=torus, in_specs=placed, out_specs=(P(ROW, COL), P()), check_vma=False
    )
```

```python
import jax
import jax.numpy as jnp
from jax import lax
from jax.experimental import pallas as pl
from jax.experimental.pallas import tpu as pltpu
from jax.sharding import Mesh
from jax.sharding import PartitionSpec as P

BS = 64
ROW = ("row_0", "row_1")
COL = ("col_0", "col_1", "col_2")
ROW_COL = ("row_0", "row_1", "col_0", "col_1", "col_2")


def tile_keep(pattern, row_index, col_index, tile_rows, tile_cols):
    row_blocks = tile_rows // BS
    span = (tile_cols + BS - 1) // BS + 1
    first_col = col_index * tile_cols
    first_block = first_col // BS
    padded = jnp.pad(pattern, ((0, 0), (0, span)))
    window = lax.dynamic_slice(padded, (row_index * row_blocks, first_block), (row_blocks, span))
    block_rows = row_index * row_blocks + jnp.arange(row_blocks, dtype=jnp.int32)[:, None]
    block_cols = first_block + jnp.arange(span, dtype=jnp.int32)[None, :]
    window = jnp.maximum(window, (block_rows == block_cols).astype(window.dtype))
    per_row = jnp.repeat(window, BS, axis=0)
    local_block = (first_col + jnp.arange(tile_cols, dtype=jnp.int32)) // BS - first_block
    keep = jnp.zeros((tile_rows, tile_cols), jnp.bool_)
    for block in range(span):
        keep = keep | ((local_block[None, :] == block) & (per_row[:, block:block + 1] > 0))
    return keep


def panel_kernel(shift_ref, left_ref, right_ref, keep_ref, square_ref, trace_ref, total_ref):
    pieces, _, depth = left_ref.shape
    total_ref[...] = jnp.dot(
        left_ref[0], right_ref[0:depth, :], preferred_element_type=jnp.float32
    )
    for piece in range(1, pieces):
        total_ref[...] += jnp.dot(
            left_ref[piece],
            right_ref[piece * depth:(piece + 1) * depth, :],
            preferred_element_type=jnp.float32,
        )
    total = total_ref[...]
    square_ref[...] = jnp.where(keep_ref[...] != 0, total, 0.0).astype(square_ref.dtype)
    rows = lax.broadcasted_iota(jnp.int32, total.shape, 0)
    cols = lax.broadcasted_iota(jnp.int32, total.shape, 1)
    diagonal = jnp.sum(jnp.where(cols - rows == shift_ref[0], total, 0.0))
    trace_ref[...] = jnp.full(trace_ref.shape, diagonal, jnp.float32)


def panel_product(shift, left, right, keep):
    pieces, tile_rows, depth = left.shape
    tile_cols = right.shape[1]
    vmem = pl.BlockSpec(memory_space=pltpu.VMEM)
    return pl.pallas_call(
        panel_kernel,
        out_shape=(
            jax.ShapeDtypeStruct((tile_rows, tile_cols), jnp.bfloat16),
            jax.ShapeDtypeStruct((8, 128), jnp.float32),
        ),
        in_specs=[pl.BlockSpec(memory_space=pltpu.SMEM), vmem, vmem, vmem],
        out_specs=(vmem, vmem),
        scratch_shapes=[pltpu.VMEM((tile_rows, tile_cols), jnp.float32)],
        cost_estimate=pl.CostEstimate(
            flops=2 * pieces * tile_rows * depth * tile_cols,
            bytes_accessed=2 * (left.size + right.size) + 6 * tile_rows * tile_cols,
            transcendentals=0,
        ),
    )(shift, left, right, keep)


def column_slab(masked):
    depth = lax.psum(1, "row_0")
    half = lax.axis_index("row_1")
    other = lax.ppermute(masked, "row_1", [(0, 1), (1, 0)])
    pair = jnp.where(
        half == 0,
        jnp.concatenate([masked, other]),
        jnp.concatenate([other, masked]),
    )
    here = lax.axis_index("row_0")
    slab = jnp.zeros((depth,) + pair.shape, pair.dtype)
    slab = lax.dynamic_update_index_in_dim(slab, pair, here, 0)
    forward = [(i, (i + 1) % depth) for i in range(depth)]
    backward = [(i, (i - 1) % depth) for i in range(depth)]
    ahead = pair
    behind = pair
    for step in range(1, depth // 2 + 1):
        ahead = lax.ppermute(ahead, "row_0", forward)
        slab = lax.dynamic_update_index_in_dim(slab, ahead, (here - step) % depth, 0)
        if step < depth - depth // 2:
            behind = lax.ppermute(behind, "row_0", backward)
            slab = lax.dynamic_update_index_in_dim(slab, behind, (here + step) % depth, 0)
    return slab.reshape(depth * pair.shape[0], pair.shape[1])


def on_device(iterate, pattern):
    tile_rows, tile_cols = iterate.shape
    nblocks = pattern.shape[0]
    order_total = nblocks * BS
    row_index = lax.axis_index(ROW)
    col_index = lax.axis_index(COL)
    keep_mask = tile_keep(pattern, row_index, col_index, tile_rows, tile_cols)
    masked = jnp.where(keep_mask, iterate, jnp.zeros((), iterate.dtype))
    left_panel = lax.all_gather(masked, COL, axis=0, tiled=False)
    right_panel = column_slab(masked)
    shift = row_index * tile_rows - col_index * tile_cols
    global_rows = jnp.arange(tile_rows, dtype=jnp.int32)[:, None]
    global_cols = jnp.arange(tile_cols, dtype=jnp.int32)[None, :]
    on_diagonal = global_cols - global_rows == shift
    trace_first = jnp.sum(
        jnp.where(on_diagonal, masked, jnp.zeros((), masked.dtype)), dtype=jnp.float32
    )
    squared, diagonal = panel_product(
        shift.reshape(1), left_panel, right_panel, keep_mask.astype(jnp.int32)
    )
    summed = jnp.stack([trace_first, diagonal[0, 0]])
    for axis in ROW_COL:
        summed = lax.psum(summed, axis)
    traces = summed / order_total
    return (squared, traces)


def solution(mesh):
    torus = Mesh(
        mesh.devices.reshape(12, 2, 4, 4, 2), ("row_0", "row_1", "col_0", "col_1", "col_2")
    )
    placed = (P(ROW, COL), P())
    return jax.shard_map(
        on_device, mesh=torus, in_specs=placed, out_specs=(P(ROW, COL), P()), check_vma=False
    )
```

```python
import jax
import jax.numpy as jnp
from jax import lax
from jax.experimental import pallas as pl
from jax.experimental.pallas import tpu as pltpu
from jax.sharding import Mesh
from jax.sharding import PartitionSpec as P

BS = 64
ROW = ("row_0", "row_1")
COL = ("col_0", "col_1", "col_2")
ROW_COL = ("row_0", "row_1", "col_0", "col_1", "col_2")


def tile_keep(pattern, row_index, col_index, tile_rows, tile_cols):
    row_blocks = tile_rows // BS
    span = (tile_cols + BS - 1) // BS + 1
    first_col = col_index * tile_cols
    first_block = first_col // BS
    padded = jnp.pad(pattern, ((0, 0), (0, span)))
    window = lax.dynamic_slice(padded, (row_index * row_blocks, first_block), (row_blocks, span))
    block_rows = row_index * row_blocks + jnp.arange(row_blocks, dtype=jnp.int32)[:, None]
    block_cols = first_block + jnp.arange(span, dtype=jnp.int32)[None, :]
    window = jnp.maximum(window, (block_rows == block_cols).astype(window.dtype))
    per_row = jnp.repeat(window, BS, axis=0)
    local_block = (first_col + jnp.arange(tile_cols, dtype=jnp.int32)) // BS - first_block
    keep = jnp.zeros((tile_rows, tile_cols), jnp.bool_)
    for block in range(span):
        keep = keep | ((local_block[None, :] == block) & (per_row[:, block:block + 1] > 0))
    return keep


def panel_kernel(
    place_ref, left_ref, right_ref, keep_ref, square_ref, trace_ref, total_ref
):
    pieces, _, depth = left_ref.shape
    total_ref[...] = jnp.dot(
        left_ref[0], right_ref[0:depth, :], preferred_element_type=jnp.float32
    )
    for piece in range(1, pieces):
        total_ref[...] += jnp.dot(
            left_ref[piece],
            right_ref[piece * depth:(piece + 1) * depth, :],
            preferred_element_type=jnp.float32,
        )
    total = total_ref[...]
    square_ref[...] = jnp.where(keep_ref[...] != 0, total, 0.0).astype(square_ref.dtype)
    rows = lax.broadcasted_iota(jnp.int32, total.shape, 0)
    cols = lax.broadcasted_iota(jnp.int32, total.shape, 1)
    on_diagonal = cols - rows == place_ref[0]
    own = left_ref[place_ref[1]].astype(jnp.float32)
    scale = 1.0 / place_ref[2].astype(jnp.float32)
    trace_ref[0] = jnp.sum(jnp.where(on_diagonal, own, 0.0)) * scale
    trace_ref[1] = jnp.sum(jnp.where(on_diagonal, total, 0.0)) * scale


def panel_product(place, left, right, keep):
    pieces, tile_rows, depth = left.shape
    tile_cols = right.shape[1]
    vmem = pl.BlockSpec(memory_space=pltpu.VMEM)
    smem = pl.BlockSpec(memory_space=pltpu.SMEM)
    return pl.pallas_call(
        panel_kernel,
        out_shape=(
            jax.ShapeDtypeStruct((tile_rows, tile_cols), jnp.bfloat16),
            jax.ShapeDtypeStruct((2,), jnp.float32),
        ),
        in_specs=[smem, vmem, vmem, vmem],
        out_specs=(vmem, smem),
        scratch_shapes=[pltpu.VMEM((tile_rows, tile_cols), jnp.float32)],
        cost_estimate=pl.CostEstimate(
            flops=2 * pieces * tile_rows * depth * tile_cols,
            bytes_accessed=2 * (left.size + right.size) + 6 * tile_rows * tile_cols,
            transcendentals=0,
        ),
    )(place, left, right, keep)


def column_slab(masked):
    depth = lax.psum(1, "row_0")
    half = lax.axis_index("row_1")
    other = lax.ppermute(masked, "row_1", [(0, 1), (1, 0)])
    pair = jnp.where(
        half == 0,
        jnp.concatenate([masked, other]),
        jnp.concatenate([other, masked]),
    )
    here = lax.axis_index("row_0")
    slab = jnp.zeros((depth,) + pair.shape, pair.dtype)
    slab = lax.dynamic_update_index_in_dim(slab, pair, here, 0)
    forward = [(i, (i + 1) % depth) for i in range(depth)]
    backward = [(i, (i - 1) % depth) for i in range(depth)]
    ahead = pair
    behind = pair
    for step in range(1, depth // 2 + 1):
        ahead = lax.ppermute(ahead, "row_0", forward)
        slab = lax.dynamic_update_index_in_dim(slab, ahead, (here - step) % depth, 0)
        if step < depth - depth // 2:
            behind = lax.ppermute(behind, "row_0", backward)
            slab = lax.dynamic_update_index_in_dim(slab, behind, (here + step) % depth, 0)
    return slab.reshape(depth * pair.shape[0], pair.shape[1])


def on_device(iterate, pattern):
    tile_rows, tile_cols = iterate.shape
    nblocks = pattern.shape[0]
    order_total = nblocks * BS
    row_index = lax.axis_index(ROW)
    col_index = lax.axis_index(COL)
    keep_mask = tile_keep(pattern, row_index, col_index, tile_rows, tile_cols)
    masked = jnp.where(keep_mask, iterate, jnp.zeros((), iterate.dtype))
    left_panel = lax.all_gather(masked, COL, axis=0, tiled=False)
    right_panel = column_slab(masked)
    shift = row_index * tile_rows - col_index * tile_cols
    place = jnp.stack([shift, col_index, jnp.int32(order_total)]).astype(jnp.int32)
    squared, traces = panel_product(
        place, left_panel, right_panel, keep_mask.astype(jnp.int32)
    )
    for axis in reversed(ROW_COL):
        traces = lax.psum(traces, axis)
    return (squared, traces)


def solution(mesh):
    torus = Mesh(
        mesh.devices.reshape(12, 2, 4, 4, 2), ("row_0", "row_1", "col_0", "col_1", "col_2")
    )
    placed = (P(ROW, COL), P())
    return jax.shard_map(
        on_device, mesh=torus, in_specs=placed, out_specs=(P(ROW, COL), P()), check_vma=False
    )
```

```python
import math

import jax
import jax.numpy as jnp
from jax import lax
from jax.experimental import pallas as pl
from jax.experimental.pallas import tpu as pltpu
from jax.sharding import Mesh
from jax.sharding import PartitionSpec as P

BS = 64
ROW = ("row_0", "row_1")
COL = ("col_0", "col_1", "col_2")
ROW_COL = ("row_0", "row_1", "col_0", "col_1", "col_2")


def tile_keep(pattern, row_index, col_index, tile_rows, tile_cols):
    row_blocks = tile_rows // BS
    span = (tile_cols + BS - 1) // BS + 1
    first_col = col_index * tile_cols
    first_block = first_col // BS
    padded = jnp.pad(pattern, ((0, 0), (0, span)))
    window = lax.dynamic_slice(padded, (row_index * row_blocks, first_block), (row_blocks, span))
    block_rows = row_index * row_blocks + jnp.arange(row_blocks, dtype=jnp.int32)[:, None]
    block_cols = first_block + jnp.arange(span, dtype=jnp.int32)[None, :]
    window = jnp.maximum(window, (block_rows == block_cols).astype(window.dtype))
    per_row = jnp.repeat(window, BS, axis=0)
    local_block = (first_col + jnp.arange(tile_cols, dtype=jnp.int32)) // BS - first_block
    keep = jnp.zeros((tile_rows, tile_cols), jnp.bool_)
    for block in range(span):
        keep = keep | ((local_block[None, :] == block) & (per_row[:, block:block + 1] > 0))
    return keep


def panel_kernel(left_ref, right_ref, keep_ref, square_ref, total_ref):
    pieces, _, depth = left_ref.shape
    total_ref[...] = jnp.dot(
        left_ref[0], right_ref[0:depth, :], preferred_element_type=jnp.float32
    )
    for piece in range(1, pieces):
        total_ref[...] += jnp.dot(
            left_ref[piece],
            right_ref[piece * depth:(piece + 1) * depth, :],
            preferred_element_type=jnp.float32,
        )
    square_ref[...] = jnp.where(keep_ref[...] != 0, total_ref[...], 0.0).astype(square_ref.dtype)


def panel_product(left, right, keep):
    pieces, tile_rows, depth = left.shape
    tile_cols = right.shape[1]
    vmem = pl.BlockSpec(memory_space=pltpu.VMEM)
    return pl.pallas_call(
        panel_kernel,
        out_shape=jax.ShapeDtypeStruct((tile_rows, tile_cols), jnp.bfloat16),
        in_specs=[vmem, vmem, vmem],
        out_specs=vmem,
        scratch_shapes=[pltpu.VMEM((tile_rows, tile_cols), jnp.float32)],
        cost_estimate=pl.CostEstimate(
            flops=2 * pieces * tile_rows * depth * tile_cols,
            bytes_accessed=2 * (left.size + right.size) + 6 * tile_rows * tile_cols,
            transcendentals=0,
        ),
    )(left, right, keep)


def local_rounds(row_group, col_group, rows_per, cols_per):
    senders = [(a, b) for a in range(row_group) for b in range(col_group)]
    edges = {}
    for a, b in senders:
        edges[(a, b)] = [
            (u, v, ((cols_per * b + v) // rows_per, (rows_per * a + u) // cols_per))
            for u in range(rows_per)
            for v in range(cols_per)
        ]
    rounds = []
    for _ in range(rows_per * cols_per):
        owner = {}

        def augment(sender, seen):
            for index, (_, _, receiver) in enumerate(edges[sender]):
                if receiver in seen:
                    continue
                seen.add(receiver)
                if receiver not in owner or augment(owner[receiver][0], seen):
                    owner[receiver] = (sender, index)
                    return True
            return False

        for sender in senders:
            if not augment(sender, set()):
                raise ValueError("no matching")
        chosen = {}
        for receiver, (sender, index) in owner.items():
            chosen[sender] = edges[sender][index]
        for sender, edge in chosen.items():
            edges[sender].remove(edge)
        rounds.append(chosen)
    return rounds


def transposed_pairs(tile, rows, cols, fine):
    tile_rows, tile_cols = tile.shape
    rows_per, cols_per = tile_rows // fine, tile_cols // fine
    super_size = math.lcm(tile_rows, tile_cols)
    row_group, col_group = super_size // tile_rows, super_size // tile_cols
    row_index = lax.axis_index(ROW)
    col_index = lax.axis_index(COL)
    local = (row_index % row_group) * col_group + col_index % col_group
    same_super = row_index // row_group == col_index // col_group
    total = jnp.zeros((), jnp.float32)
    for chosen in local_rounds(row_group, col_group, rows_per, cols_per):
        send_u, send_v, recv_u, recv_v, to_self = [], [], [], [], []
        by_receiver = {}
        for (a, b), (u, v, (a2, b2)) in sorted(chosen.items()):
            by_receiver[(a2, b2)] = (cols_per * b + v - rows_per * a2, rows_per * a + u - cols_per * b2)
        for a in range(row_group):
            for b in range(col_group):
                u, v, (a2, b2) = chosen[(a, b)]
                send_u.append(u)
                send_v.append(v)
                recv_u.append(by_receiver[(a, b)][0])
                recv_v.append(by_receiver[(a, b)][1])
                to_self.append((a2, b2) == (a, b))
        pairs = []
        for r in range(rows):
            for c in range(cols):
                big_i, a = divmod(r, row_group)
                big_j, b = divmod(c, col_group)
                u, v, (a2, b2) = chosen[(a, b)]
                dest = (big_j * row_group + a2) * cols + big_i * col_group + b2
                if dest != r * cols + c:
                    pairs.append((r * cols + c, dest))
        pick = lambda table: jnp.asarray(table, jnp.int32)[local]
        block = lax.dynamic_slice(
            tile, (pick(send_u) * fine, pick(send_v) * fine), (fine, fine)
        )
        got = lax.ppermute(block, ROW_COL, pairs)
        got = jnp.where(same_super & jnp.asarray(to_self)[local], block, got)
        mine = lax.dynamic_slice(
            tile, (pick(recv_u) * fine, pick(recv_v) * fine), (fine, fine)
        )
        total = total + jnp.sum(mine.astype(jnp.float32) * got.astype(jnp.float32).T)
    return total


def exchange(value, axis, size, stride, group):
    position = (lax.axis_index(axis) // stride) % group
    received = [value]
    for shift in range(1, group):
        pairs = []
        for i in range(size):
            here = (i // stride) % group
            pairs.append((i, i + stride * ((here + shift) % group - here)))
        received.append(lax.ppermute(value, axis, pairs))
    total = None
    for origin in range(group):
        pick = received[0]
        for here in range(group):
            pick = jnp.where(position == here, received[(here - origin) % group], pick)
        total = pick if total is None else total + pick
    return total


def reduction_stages():
    stages = []
    for axis, size in (("col_2", 2), ("col_1", 4), ("col_0", 4), ("row_1", 2), ("row_0", 12)):
        stride = 1
        for group in (4, 3, 2):
            while size % (stride * group) == 0 and stride * group <= size:
                stages.append((axis, size, stride, group))
                stride *= group
    return stages


def column_slab(masked, partial, stages):
    depth = lax.psum(1, "row_0")
    half = lax.axis_index("row_1")
    other = lax.ppermute(masked, "row_1", [(0, 1), (1, 0)])
    pair = jnp.where(
        half == 0,
        jnp.concatenate([masked, other]),
        jnp.concatenate([other, masked]),
    )
    here = lax.axis_index("row_0")
    slab = jnp.zeros((depth,) + pair.shape, pair.dtype)
    slab = lax.dynamic_update_index_in_dim(slab, pair, here, 0)
    forward = [(i, (i + 1) % depth) for i in range(depth)]
    backward = [(i, (i - 1) % depth) for i in range(depth)]
    ahead = pair
    behind = pair
    for step in range(1, depth // 2 + 1):
        ahead = lax.ppermute(ahead, "row_0", forward)
        if step < depth - depth // 2:
            behind = lax.ppermute(behind, "row_0", backward)
        if stages:
            partial = exchange(partial, *stages.pop(0))
        ahead, behind, partial = lax.optimization_barrier((ahead, behind, partial))
        slab = lax.dynamic_update_index_in_dim(slab, ahead, (here - step) % depth, 0)
        if step < depth - depth // 2:
            slab = lax.dynamic_update_index_in_dim(slab, behind, (here + step) % depth, 0)
    for stage in stages:
        partial = exchange(partial, *stage)
    return slab.reshape(depth * pair.shape[0], pair.shape[1]), partial


def on_device(iterate, pattern):
    tile_rows, tile_cols = iterate.shape
    nblocks = pattern.shape[0]
    order_total = nblocks * BS
    row_index = lax.axis_index(ROW)
    col_index = lax.axis_index(COL)
    keep_mask = tile_keep(pattern, row_index, col_index, tile_rows, tile_cols)
    masked = jnp.where(keep_mask, iterate, jnp.zeros((), iterate.dtype))
    left_panel = lax.all_gather(masked, COL, axis=0, tiled=False)
    shift = row_index * tile_rows - col_index * tile_cols
    rows_local = jnp.arange(tile_rows, dtype=jnp.int32)[:, None]
    cols_local = jnp.arange(tile_cols, dtype=jnp.int32)[None, :]
    on_diagonal = cols_local - rows_local == shift
    trace_first = jnp.sum(
        jnp.where(on_diagonal, masked, jnp.zeros((), masked.dtype)), dtype=jnp.float32
    )
    rows, cols = lax.psum(1, ROW), lax.psum(1, COL)
    trace_second = transposed_pairs(masked, rows, cols, math.gcd(tile_rows, tile_cols))
    partial = jnp.stack([trace_first, trace_second])
    right_panel, summed = column_slab(masked, partial, reduction_stages())
    squared = panel_product(left_panel, right_panel, keep_mask.astype(jnp.int32))
    traces = summed / order_total
    return (squared, traces)


def solution(mesh):
    torus = Mesh(
        mesh.devices.reshape(12, 2, 4, 4, 2), ("row_0", "row_1", "col_0", "col_1", "col_2")
    )
    placed = (P(ROW, COL), P())
    return jax.shard_map(
        on_device, mesh=torus, in_specs=placed, out_specs=(P(ROW, COL), P()), check_vma=False
    )
```

```python
import jax
import jax.numpy as jnp
from jax import lax
from jax.experimental import pallas as pl
from jax.experimental.pallas import tpu as pltpu
from jax.sharding import Mesh
from jax.sharding import PartitionSpec as P

BS = 64
ROW = ("row_0", "row_1")
COL = ("col_0", "col_1", "col_2")
ROW_COL = ("row_0", "row_1", "col_0", "col_1", "col_2")


def tile_keep(pattern, row_index, col_index, tile_rows, tile_cols):
    row_blocks = tile_rows // BS
    span = (tile_cols + BS - 1) // BS + 1
    first_col = col_index * tile_cols
    first_block = first_col // BS
    padded = jnp.pad(pattern, ((0, 0), (0, span)))
    window = lax.dynamic_slice(padded, (row_index * row_blocks, first_block), (row_blocks, span))
    block_rows = row_index * row_blocks + jnp.arange(row_blocks, dtype=jnp.int32)[:, None]
    block_cols = first_block + jnp.arange(span, dtype=jnp.int32)[None, :]
    window = jnp.maximum(window, (block_rows == block_cols).astype(window.dtype))
    per_row = jnp.repeat(window, BS, axis=0)
    local_block = (first_col + jnp.arange(tile_cols, dtype=jnp.int32)) // BS - first_block
    keep = jnp.zeros((tile_rows, tile_cols), jnp.bool_)
    for block in range(span):
        keep = keep | ((local_block[None, :] == block) & (per_row[:, block:block + 1] > 0))
    return keep


def panel_kernel(
    place_ref, left_ref, right_ref, keep_ref, square_ref, trace_ref, total_ref
):
    pieces, tile_rows, depth = left_ref.shape
    chunk = tile_rows // 2
    first = jnp.zeros((), jnp.float32)
    second = jnp.zeros((), jnp.float32)
    for start in range(0, tile_rows, chunk):
        rows = slice(start, start + chunk)
        total = jnp.dot(
            left_ref[0, rows, :], right_ref[0:depth, :], preferred_element_type=jnp.float32
        )
        for piece in range(1, pieces):
            total = total + jnp.dot(
                left_ref[piece, rows, :],
                right_ref[piece * depth:(piece + 1) * depth, :],
                preferred_element_type=jnp.float32,
            )
        square_ref[rows, :] = jnp.where(keep_ref[rows, :] != 0, total, 0.0).astype(
            square_ref.dtype
        )
        local_rows = lax.broadcasted_iota(jnp.int32, total.shape, 0) + start
        cols = lax.broadcasted_iota(jnp.int32, total.shape, 1)
        on_diagonal = cols - local_rows == place_ref[0]
        own = left_ref[place_ref[1], rows, :].astype(jnp.float32)
        first = first + jnp.sum(jnp.where(on_diagonal, own, 0.0))
        second = second + jnp.sum(jnp.where(on_diagonal, total, 0.0))
    scale = 1.0 / place_ref[2].astype(jnp.float32)
    trace_ref[0] = first * scale
    trace_ref[1] = second * scale


def panel_product(place, left, right, keep):
    pieces, tile_rows, depth = left.shape
    tile_cols = right.shape[1]
    vmem = pl.BlockSpec(memory_space=pltpu.VMEM)
    smem = pl.BlockSpec(memory_space=pltpu.SMEM)
    return pl.pallas_call(
        panel_kernel,
        out_shape=(
            jax.ShapeDtypeStruct((tile_rows, tile_cols), jnp.bfloat16),
            jax.ShapeDtypeStruct((2,), jnp.float32),
        ),
        in_specs=[smem, vmem, vmem, vmem],
        out_specs=(vmem, smem),
        scratch_shapes=[pltpu.VMEM((tile_rows, tile_cols), jnp.float32)],
        cost_estimate=pl.CostEstimate(
            flops=2 * pieces * tile_rows * depth * tile_cols,
            bytes_accessed=2 * (left.size + right.size) + 6 * tile_rows * tile_cols,
            transcendentals=0,
        ),
    )(place, left, right, keep)


def column_slab(masked):
    depth = lax.psum(1, "row_0")
    half = lax.axis_index("row_1")
    other = lax.ppermute(masked, "row_1", [(0, 1), (1, 0)])
    pair = jnp.where(
        half == 0,
        jnp.concatenate([masked, other]),
        jnp.concatenate([other, masked]),
    )
    here = lax.axis_index("row_0")
    slab = jnp.zeros((depth,) + pair.shape, pair.dtype)
    slab = lax.dynamic_update_index_in_dim(slab, pair, here, 0)
    forward = [(i, (i + 1) % depth) for i in range(depth)]
    backward = [(i, (i - 1) % depth) for i in range(depth)]
    ahead = pair
    behind = pair
    for step in range(1, depth // 2 + 1):
        ahead = lax.ppermute(ahead, "row_0", forward)
        slab = lax.dynamic_update_index_in_dim(slab, ahead, (here - step) % depth, 0)
        if step < depth - depth // 2:
            behind = lax.ppermute(behind, "row_0", backward)
            slab = lax.dynamic_update_index_in_dim(slab, behind, (here + step) % depth, 0)
    return slab.reshape(depth * pair.shape[0], pair.shape[1])


def on_device(iterate, pattern):
    tile_rows, tile_cols = iterate.shape
    nblocks = pattern.shape[0]
    order_total = nblocks * BS
    row_index = lax.axis_index(ROW)
    col_index = lax.axis_index(COL)
    keep_mask = tile_keep(pattern, row_index, col_index, tile_rows, tile_cols)
    masked = jnp.where(keep_mask, iterate, jnp.zeros((), iterate.dtype))
    left_panel = lax.all_gather(masked, COL, axis=0, tiled=False)
    right_panel = column_slab(masked)
    shift = row_index * tile_rows - col_index * tile_cols
    place = jnp.stack([shift, col_index, jnp.int32(order_total)]).astype(jnp.int32)
    squared, traces = panel_product(
        place, left_panel, right_panel, keep_mask.astype(jnp.int32)
    )
    for axis in reversed(ROW_COL):
        traces = lax.psum(traces, axis)
    return (squared, traces)


def solution(mesh):
    torus = Mesh(
        mesh.devices.reshape(12, 2, 4, 4, 2), ("row_0", "row_1", "col_0", "col_1", "col_2")
    )
    placed = (P(ROW, COL), P())
    return jax.shard_map(
        on_device, mesh=torus, in_specs=placed, out_specs=(P(ROW, COL), P()), check_vma=False
    )
```

```python
import jax
import jax.numpy as jnp
from jax import lax
from jax.experimental import pallas as pl
from jax.experimental.pallas import tpu as pltpu
from jax.sharding import Mesh
from jax.sharding import PartitionSpec as P

BS = 64
ROW = ("row_0", "row_1")
COL = ("col_0", "col_1", "col_2")
ROW_COL = ("row_0", "row_1", "col_0", "col_1", "col_2")


def tile_keep(pattern, row_index, col_index, tile_rows, tile_cols):
    row_blocks = tile_rows // BS
    span = (tile_cols + BS - 1) // BS + 1
    first_col = col_index * tile_cols
    first_block = first_col // BS
    padded = jnp.pad(pattern, ((0, 0), (0, span)))
    window = lax.dynamic_slice(padded, (row_index * row_blocks, first_block), (row_blocks, span))
    block_rows = row_index * row_blocks + jnp.arange(row_blocks, dtype=jnp.int32)[:, None]
    block_cols = first_block + jnp.arange(span, dtype=jnp.int32)[None, :]
    window = jnp.maximum(window, (block_rows == block_cols).astype(window.dtype))
    per_row = jnp.repeat(window, BS, axis=0)
    local_block = (first_col + jnp.arange(tile_cols, dtype=jnp.int32)) // BS - first_block
    keep = jnp.zeros((tile_rows, tile_cols), jnp.bool_)
    for block in range(span):
        keep = keep | ((local_block[None, :] == block) & (per_row[:, block:block + 1] > 0))
    return keep


def panel_kernel(
    place_ref, left_ref, right_ref, keep_ref, square_ref, trace_ref, total_ref
):
    pieces, tile_rows, depth = left_ref.shape
    chunk = tile_rows // 2
    first = jnp.zeros((), jnp.float32)
    second = jnp.zeros((), jnp.float32)
    for start in range(0, tile_rows, chunk):
        rows = slice(start, start + chunk)
        total = jnp.dot(
            left_ref[0, rows, :], right_ref[0:depth, :], preferred_element_type=jnp.float32
        )
        for piece in range(1, pieces):
            total = total + jnp.dot(
                left_ref[piece, rows, :],
                right_ref[piece * depth:(piece + 1) * depth, :],
                preferred_element_type=jnp.float32,
            )
        square_ref[rows, :] = jnp.where(keep_ref[rows, :] != 0, total, 0.0).astype(
            square_ref.dtype
        )
        local_rows = lax.broadcasted_iota(jnp.int32, total.shape, 0) + start
        cols = lax.broadcasted_iota(jnp.int32, total.shape, 1)
        on_diagonal = cols - local_rows == place_ref[0]
        own = left_ref[place_ref[1], rows, :].astype(jnp.float32)
        first = first + jnp.sum(jnp.where(on_diagonal, own, 0.0))
        second = second + jnp.sum(jnp.where(on_diagonal, total, 0.0))
    scale = 1.0 / place_ref[2].astype(jnp.float32)
    trace_ref[0] = first * scale
    trace_ref[1] = second * scale


def panel_product(place, left, right, keep):
    pieces, tile_rows, depth = left.shape
    tile_cols = right.shape[1]
    vmem = pl.BlockSpec(memory_space=pltpu.VMEM)
    smem = pl.BlockSpec(memory_space=pltpu.SMEM)
    return pl.pallas_call(
        panel_kernel,
        out_shape=(
            jax.ShapeDtypeStruct((tile_rows, tile_cols), jnp.bfloat16),
            jax.ShapeDtypeStruct((2,), jnp.float32),
        ),
        in_specs=[smem, vmem, vmem, vmem],
        out_specs=(vmem, smem),
        scratch_shapes=[pltpu.VMEM((tile_rows, tile_cols), jnp.float32)],
        cost_estimate=pl.CostEstimate(
            flops=2 * pieces * tile_rows * depth * tile_cols,
            bytes_accessed=2 * (left.size + right.size) + 6 * tile_rows * tile_cols,
            transcendentals=0,
        ),
    )(place, left, right, keep)


def ring_chain(own, partner, slab, here, depth, count, sign):
    rows = own.shape[0]
    half = lax.axis_index("row_1")
    perm = [(i, (i + sign) % depth) for i in range(depth)]
    received = None
    for step in range(1, count + 2):
        if step == 1:
            message = own
        elif step == 2:
            message = jnp.concatenate([received, partner])
        elif step <= count:
            message = received
        else:
            message = received[rows:]
        received = lax.ppermute(message, "row_0", perm)
        own_at = (here - sign * step) % depth
        partner_at = (here - sign * (step - 1)) % depth
        if step <= count:
            slab = lax.dynamic_update_slice(
                slab, received[None, None, :rows], (own_at, half, 0, 0)
            )
        if step >= 2:
            slab = lax.dynamic_update_slice(
                slab, received[None, None, -rows:], (partner_at, 1 - half, 0, 0)
            )
    return slab


def column_slab(masked):
    depth = lax.psum(1, "row_0")
    half = lax.axis_index("row_1")
    partner = lax.ppermute(masked, "row_1", [(0, 1), (1, 0)])
    here = lax.axis_index("row_0")
    slab = jnp.zeros((depth, 2) + masked.shape, masked.dtype)
    slab = lax.dynamic_update_slice(slab, masked[None, None], (here, half, 0, 0))
    slab = lax.dynamic_update_slice(slab, partner[None, None], (here, 1 - half, 0, 0))
    slab = ring_chain(masked, partner, slab, here, depth, depth // 2, 1)
    slab = ring_chain(masked, partner, slab, here, depth, depth - 1 - depth // 2, -1)
    return slab.reshape(depth * 2 * masked.shape[0], masked.shape[1])


def on_device(iterate, pattern):
    tile_rows, tile_cols = iterate.shape
    nblocks = pattern.shape[0]
    order_total = nblocks * BS
    row_index = lax.axis_index(ROW)
    col_index = lax.axis_index(COL)
    keep_mask = tile_keep(pattern, row_index, col_index, tile_rows, tile_cols)
    masked = jnp.where(keep_mask, iterate, jnp.zeros((), iterate.dtype))
    left_panel = lax.all_gather(masked, COL, axis=0, tiled=False)
    right_panel = column_slab(masked)
    shift = row_index * tile_rows - col_index * tile_cols
    place = jnp.stack([shift, col_index, jnp.int32(order_total)]).astype(jnp.int32)
    squared, traces = panel_product(
        place, left_panel, right_panel, keep_mask.astype(jnp.int32)
    )
    for axis in reversed(ROW_COL):
        traces = lax.psum(traces, axis)
    return (squared, traces)


def solution(mesh):
    torus = Mesh(
        mesh.devices.reshape(12, 2, 4, 4, 2), ("row_0", "row_1", "col_0", "col_1", "col_2")
    )
    placed = (P(ROW, COL), P())
    return jax.shard_map(
        on_device, mesh=torus, in_specs=placed, out_specs=(P(ROW, COL), P()), check_vma=False
    )
```

```python
import jax
import jax.numpy as jnp
from jax import lax
from jax.experimental import pallas as pl
from jax.experimental.pallas import tpu as pltpu
from jax.sharding import Mesh
from jax.sharding import PartitionSpec as P

BS = 64
ROW = ("row_0", "row_1")
COL = ("col_0", "col_1", "col_2")
ROW_COL = ("row_0", "row_1", "col_0", "col_1", "col_2")


def tile_keep(pattern, row_index, col_index, tile_rows, tile_cols):
    row_blocks = tile_rows // BS
    span = (tile_cols + BS - 1) // BS + 1
    first_col = col_index * tile_cols
    first_block = first_col // BS
    padded = jnp.pad(pattern, ((0, 0), (0, span)))
    window = lax.dynamic_slice(padded, (row_index * row_blocks, first_block), (row_blocks, span))
    block_rows = row_index * row_blocks + jnp.arange(row_blocks, dtype=jnp.int32)[:, None]
    block_cols = first_block + jnp.arange(span, dtype=jnp.int32)[None, :]
    window = jnp.maximum(window, (block_rows == block_cols).astype(window.dtype))
    bits = jnp.sum(
        (window > 0).astype(jnp.int32) << jnp.arange(span, dtype=jnp.int32)[None, :], axis=1
    )
    per_row = jnp.repeat(bits, BS)[:, None]
    local_block = (first_col + jnp.arange(tile_cols, dtype=jnp.int32)) // BS - first_block
    return ((per_row >> local_block[None, :]) & 1) > 0


def panel_kernel(
    place_ref, left_ref, right_ref, keep_ref, square_ref, trace_ref, total_ref
):
    pieces, tile_rows, depth = left_ref.shape
    chunk = tile_rows // 2
    first = jnp.zeros((), jnp.float32)
    second = jnp.zeros((), jnp.float32)
    for start in range(0, tile_rows, chunk):
        rows = slice(start, start + chunk)
        total = jnp.dot(
            left_ref[0, rows, :], right_ref[0:depth, :], preferred_element_type=jnp.float32
        )
        for piece in range(1, pieces):
            total = total + jnp.dot(
                left_ref[piece, rows, :],
                right_ref[piece * depth:(piece + 1) * depth, :],
                preferred_element_type=jnp.float32,
            )
        square_ref[rows, :] = jnp.where(keep_ref[rows, :] != 0, total, 0.0).astype(
            square_ref.dtype
        )
        local_rows = lax.broadcasted_iota(jnp.int32, total.shape, 0) + start
        cols = lax.broadcasted_iota(jnp.int32, total.shape, 1)
        on_diagonal = cols - local_rows == place_ref[0]
        own = left_ref[place_ref[1], rows, :].astype(jnp.float32)
        first = first + jnp.sum(jnp.where(on_diagonal, own, 0.0))
        second = second + jnp.sum(jnp.where(on_diagonal, total, 0.0))
    scale = 1.0 / place_ref[2].astype(jnp.float32)
    trace_ref[0] = first * scale
    trace_ref[1] = second * scale


def panel_product(place, left, right, keep):
    pieces, tile_rows, depth = left.shape
    tile_cols = right.shape[1]
    vmem = pl.BlockSpec(memory_space=pltpu.VMEM)
    smem = pl.BlockSpec(memory_space=pltpu.SMEM)
    return pl.pallas_call(
        panel_kernel,
        out_shape=(
            jax.ShapeDtypeStruct((tile_rows, tile_cols), jnp.bfloat16),
            jax.ShapeDtypeStruct((2,), jnp.float32),
        ),
        in_specs=[smem, vmem, vmem, vmem],
        out_specs=(vmem, smem),
        scratch_shapes=[pltpu.VMEM((tile_rows, tile_cols), jnp.float32)],
        cost_estimate=pl.CostEstimate(
            flops=2 * pieces * tile_rows * depth * tile_cols,
            bytes_accessed=2 * (left.size + right.size) + 6 * tile_rows * tile_cols,
            transcendentals=0,
        ),
    )(place, left, right, keep)


def column_slab(masked):
    depth = lax.psum(1, "row_0")
    half = lax.axis_index("row_1")
    other = lax.ppermute(masked, "row_1", [(0, 1), (1, 0)])
    pair = jnp.where(
        half == 0,
        jnp.concatenate([masked, other]),
        jnp.concatenate([other, masked]),
    )
    here = lax.axis_index("row_0")
    slab = jnp.zeros((depth,) + pair.shape, pair.dtype)
    slab = lax.dynamic_update_index_in_dim(slab, pair, here, 0)
    forward = [(i, (i + 1) % depth) for i in range(depth)]
    backward = [(i, (i - 1) % depth) for i in range(depth)]
    ahead = pair
    behind = pair
    for step in range(1, depth // 2 + 1):
        ahead = lax.ppermute(ahead, "row_0", forward)
        slab = lax.dynamic_update_index_in_dim(slab, ahead, (here - step) % depth, 0)
        if step < depth - depth // 2:
            behind = lax.ppermute(behind, "row_0", backward)
            slab = lax.dynamic_update_index_in_dim(slab, behind, (here + step) % depth, 0)
    return slab.reshape(depth * pair.shape[0], pair.shape[1])


def on_device(iterate, pattern):
    tile_rows, tile_cols = iterate.shape
    nblocks = pattern.shape[0]
    order_total = nblocks * BS
    row_index = lax.axis_index(ROW)
    col_index = lax.axis_index(COL)
    keep_mask = tile_keep(pattern, row_index, col_index, tile_rows, tile_cols)
    masked = jnp.where(keep_mask, iterate, jnp.zeros((), iterate.dtype))
    left_panel = lax.all_gather(masked, COL, axis=0, tiled=False)
    right_panel = column_slab(masked)
    shift = row_index * tile_rows - col_index * tile_cols
    place = jnp.stack([shift, col_index, jnp.int32(order_total)]).astype(jnp.int32)
    squared, traces = panel_product(
        place, left_panel, right_panel, keep_mask.astype(jnp.int32)
    )
    for axis in reversed(ROW_COL):
        traces = lax.psum(traces, axis)
    return (squared, traces)


def solution(mesh):
    torus = Mesh(
        mesh.devices.reshape(12, 2, 4, 4, 2), ("row_0", "row_1", "col_0", "col_1", "col_2")
    )
    placed = (P(ROW, COL), P())
    return jax.shard_map(
        on_device, mesh=torus, in_specs=placed, out_specs=(P(ROW, COL), P()), check_vma=False
    )
```

```python
import jax
import jax.numpy as jnp
from jax import lax
from jax.experimental import pallas as pl
from jax.experimental.pallas import tpu as pltpu
from jax.sharding import Mesh
from jax.sharding import PartitionSpec as P

BS = 64
ROW = ("row_0", "row_1")
COL = ("col_0", "col_1", "col_2")
ROW_COL = ("row_0", "row_1", "col_0", "col_1", "col_2")


def tile_keep(pattern, row_index, col_index, tile_rows, tile_cols):
    row_blocks = tile_rows // BS
    span = (tile_cols + BS - 1) // BS + 1
    first_col = col_index * tile_cols
    first_block = first_col // BS
    padded = jnp.pad(pattern, ((0, 0), (0, span)))
    window = lax.dynamic_slice(padded, (row_index * row_blocks, first_block), (row_blocks, span))
    block_rows = row_index * row_blocks + jnp.arange(row_blocks, dtype=jnp.int32)[:, None]
    block_cols = first_block + jnp.arange(span, dtype=jnp.int32)[None, :]
    window = jnp.maximum(window, (block_rows == block_cols).astype(window.dtype))
    bits = jnp.sum(
        (window > 0).astype(jnp.int32) << jnp.arange(span, dtype=jnp.int32)[None, :], axis=1
    )
    per_row = jnp.repeat(bits, BS)[:, None]
    local_block = (first_col + jnp.arange(tile_cols, dtype=jnp.int32)) // BS - first_block
    return ((per_row >> local_block[None, :]) & 1) > 0


def panel_kernel(
    place_ref, left_ref, right_ref, keep_ref, square_ref, trace_ref, total_ref
):
    pieces, tile_rows, depth = left_ref.shape
    chunk = tile_rows // 2
    first = jnp.zeros((), jnp.float32)
    second = jnp.zeros((), jnp.float32)
    for start in range(0, tile_rows, chunk):
        rows = slice(start, start + chunk)
        total = jnp.dot(
            left_ref[0, rows, :], right_ref[0:depth, :], preferred_element_type=jnp.float32
        )
        for piece in range(1, pieces):
            total = total + jnp.dot(
                left_ref[piece, rows, :],
                right_ref[piece * depth:(piece + 1) * depth, :],
                preferred_element_type=jnp.float32,
            )
        square_ref[rows, :] = jnp.where(keep_ref[rows, :] != 0, total, 0.0).astype(
            square_ref.dtype
        )
        local_rows = lax.broadcasted_iota(jnp.int32, total.shape, 0) + start
        cols = lax.broadcasted_iota(jnp.int32, total.shape, 1)
        on_diagonal = cols - local_rows == place_ref[0]
        own = left_ref[place_ref[1], rows, :].astype(jnp.float32)
        first = first + jnp.sum(jnp.where(on_diagonal, own, 0.0))
        second = second + jnp.sum(jnp.where(on_diagonal, total, 0.0))
    scale = 1.0 / place_ref[2].astype(jnp.float32)
    trace_ref[0] = first * scale
    trace_ref[1] = second * scale


def panel_product(place, left, right, keep):
    pieces, tile_rows, depth = left.shape
    tile_cols = right.shape[1]
    vmem = pl.BlockSpec(memory_space=pltpu.VMEM)
    smem = pl.BlockSpec(memory_space=pltpu.SMEM)
    return pl.pallas_call(
        panel_kernel,
        out_shape=(
            jax.ShapeDtypeStruct((tile_rows, tile_cols), jnp.bfloat16),
            jax.ShapeDtypeStruct((2,), jnp.float32),
        ),
        in_specs=[smem, vmem, vmem, vmem],
        out_specs=(vmem, smem),
        scratch_shapes=[pltpu.VMEM((tile_rows, tile_cols), jnp.float32)],
        cost_estimate=pl.CostEstimate(
            flops=2 * pieces * tile_rows * depth * tile_cols,
            bytes_accessed=2 * (left.size + right.size) + 6 * tile_rows * tile_cols,
            transcendentals=0,
        ),
    )(place, left, right, keep)


def column_slab(masked):
    depth = lax.psum(1, "row_0")
    half = lax.axis_index("row_1")
    other = lax.ppermute(masked, "row_1", [(0, 1), (1, 0)])
    pair = jnp.where(
        half == 0,
        jnp.concatenate([masked, other]),
        jnp.concatenate([other, masked]),
    )
    here = lax.axis_index("row_0")
    slab = jnp.zeros((depth,) + pair.shape, pair.dtype)
    slab = lax.dynamic_update_index_in_dim(slab, pair, here, 0)
    forward = [(i, (i + 1) % depth) for i in range(depth)]
    backward = [(i, (i - 1) % depth) for i in range(depth)]
    ahead = pair
    behind = pair
    last = depth // 2
    split = depth % 2 == 0
    for step in range(1, last + 1):
        if split and step == last:
            rows = masked.shape[0]
            top = lax.ppermute(ahead[:rows], "row_0", forward)
            bottom = lax.ppermute(behind[rows:], "row_0", backward)
            at = (here - step) % depth
            slab = lax.dynamic_update_slice(slab, top[None], (at, 0, 0))
            slab = lax.dynamic_update_slice(slab, bottom[None], (at, rows, 0))
            continue
        ahead = lax.ppermute(ahead, "row_0", forward)
        slab = lax.dynamic_update_index_in_dim(slab, ahead, (here - step) % depth, 0)
        if step < depth - depth // 2:
            behind = lax.ppermute(behind, "row_0", backward)
            slab = lax.dynamic_update_index_in_dim(slab, behind, (here + step) % depth, 0)
    return slab.reshape(depth * pair.shape[0], pair.shape[1])


def on_device(iterate, pattern):
    tile_rows, tile_cols = iterate.shape
    nblocks = pattern.shape[0]
    order_total = nblocks * BS
    row_index = lax.axis_index(ROW)
    col_index = lax.axis_index(COL)
    keep_mask = tile_keep(pattern, row_index, col_index, tile_rows, tile_cols)
    masked = jnp.where(keep_mask, iterate, jnp.zeros((), iterate.dtype))
    left_panel = lax.all_gather(masked, COL, axis=0, tiled=False)
    right_panel = column_slab(masked)
    shift = row_index * tile_rows - col_index * tile_cols
    place = jnp.stack([shift, col_index, jnp.int32(order_total)]).astype(jnp.int32)
    squared, traces = panel_product(
        place, left_panel, right_panel, keep_mask.astype(jnp.int32)
    )
    for axis in reversed(ROW_COL):
        traces = lax.psum(traces, axis)
    return (squared, traces)


def solution(mesh):
    torus = Mesh(
        mesh.devices.reshape(12, 2, 4, 4, 2), ("row_0", "row_1", "col_0", "col_1", "col_2")
    )
    placed = (P(ROW, COL), P())
    return jax.shard_map(
        on_device, mesh=torus, in_specs=placed, out_specs=(P(ROW, COL), P()), check_vma=False
    )
```

```python
import jax
import jax.numpy as jnp
from jax import lax
from jax.experimental import pallas as pl
from jax.experimental.pallas import tpu as pltpu
from jax.sharding import Mesh
from jax.sharding import PartitionSpec as P

BS = 64
ROW = ("row_0", "row_1")
COL = ("col_0", "col_1", "col_2")
ROW_COL = ("row_0", "row_1", "col_0", "col_1", "col_2")


def tile_keep(pattern, row_index, col_index, tile_rows, tile_cols):
    row_blocks = tile_rows // BS
    span = (tile_cols + BS - 1) // BS + 1
    first_col = col_index * tile_cols
    first_block = first_col // BS
    padded = jnp.pad(pattern, ((0, 0), (0, span)))
    window = lax.dynamic_slice(padded, (row_index * row_blocks, first_block), (row_blocks, span))
    block_rows = row_index * row_blocks + jnp.arange(row_blocks, dtype=jnp.int32)[:, None]
    block_cols = first_block + jnp.arange(span, dtype=jnp.int32)[None, :]
    window = jnp.maximum(window, (block_rows == block_cols).astype(window.dtype))
    bits = jnp.sum(
        (window > 0).astype(jnp.int32) << jnp.arange(span, dtype=jnp.int32)[None, :], axis=1
    )
    per_row = jnp.repeat(bits, BS)[:, None]
    local_block = (first_col + jnp.arange(tile_cols, dtype=jnp.int32)) // BS - first_block
    return ((per_row >> local_block[None, :]) & 1) > 0


def panel_kernel(
    place_ref, left_ref, right_ref, keep_ref, square_ref, trace_ref, total_ref
):
    pieces, tile_rows, depth = left_ref.shape
    chunk = tile_rows // 2
    first = jnp.zeros((), jnp.float32)
    second = jnp.zeros((), jnp.float32)
    for start in range(0, tile_rows, chunk):
        rows = slice(start, start + chunk)
        total = jnp.dot(
            left_ref[0, rows, :], right_ref[0:depth, :], preferred_element_type=jnp.float32
        )
        for piece in range(1, pieces):
            total = total + jnp.dot(
                left_ref[piece, rows, :],
                right_ref[piece * depth:(piece + 1) * depth, :],
                preferred_element_type=jnp.float32,
            )
        square_ref[rows, :] = jnp.where(keep_ref[rows, :] != 0, total, 0.0).astype(
            square_ref.dtype
        )
        local_rows = lax.broadcasted_iota(jnp.int32, total.shape, 0) + start
        cols = lax.broadcasted_iota(jnp.int32, total.shape, 1)
        on_diagonal = cols - local_rows == place_ref[0]
        own = left_ref[place_ref[1], rows, :].astype(jnp.float32)
        first = first + jnp.sum(jnp.where(on_diagonal, own, 0.0))
        second = second + jnp.sum(jnp.where(on_diagonal, total, 0.0))
    scale = 1.0 / place_ref[2].astype(jnp.float32)
    trace_ref[0] = first * scale
    trace_ref[1] = second * scale


def panel_product(place, left, right, keep):
    pieces, tile_rows, depth = left.shape
    tile_cols = right.shape[1]
    vmem = pl.BlockSpec(memory_space=pltpu.VMEM)
    smem = pl.BlockSpec(memory_space=pltpu.SMEM)
    return pl.pallas_call(
        panel_kernel,
        out_shape=(
            jax.ShapeDtypeStruct((tile_rows, tile_cols), jnp.bfloat16),
            jax.ShapeDtypeStruct((2,), jnp.float32),
        ),
        in_specs=[smem, vmem, vmem, vmem],
        out_specs=(vmem, smem),
        scratch_shapes=[pltpu.VMEM((tile_rows, tile_cols), jnp.float32)],
        cost_estimate=pl.CostEstimate(
            flops=2 * pieces * tile_rows * depth * tile_cols,
            bytes_accessed=2 * (left.size + right.size) + 6 * tile_rows * tile_cols,
            transcendentals=0,
        ),
    )(place, left, right, keep)


def column_slab(masked):
    depth = lax.psum(1, "row_0")
    half = lax.axis_index("row_1")
    other = lax.ppermute(masked, "row_1", [(0, 1), (1, 0)])
    pair = jnp.where(
        half == 0,
        jnp.concatenate([masked, other]),
        jnp.concatenate([other, masked]),
    )
    here = lax.axis_index("row_0")
    slab = jnp.zeros((depth,) + pair.shape, pair.dtype)
    slab = lax.dynamic_update_index_in_dim(slab, pair, here, 0)
    forward = [(i, (i + 1) % depth) for i in range(depth)]
    backward = [(i, (i - 1) % depth) for i in range(depth)]
    ahead = pair
    behind = pair
    for step in range(1, depth // 2 + 1):
        if step < depth - depth // 2:
            behind = lax.ppermute(behind, "row_0", backward)
            slab = lax.dynamic_update_index_in_dim(slab, behind, (here + step) % depth, 0)
        ahead = lax.ppermute(ahead, "row_0", forward)
        slab = lax.dynamic_update_index_in_dim(slab, ahead, (here - step) % depth, 0)
    return slab.reshape(depth * pair.shape[0], pair.shape[1])


def on_device(iterate, pattern):
    tile_rows, tile_cols = iterate.shape
    nblocks = pattern.shape[0]
    order_total = nblocks * BS
    row_index = lax.axis_index(ROW)
    col_index = lax.axis_index(COL)
    keep_mask = tile_keep(pattern, row_index, col_index, tile_rows, tile_cols)
    masked = jnp.where(keep_mask, iterate, jnp.zeros((), iterate.dtype))
    left_panel = lax.all_gather(masked, COL, axis=0, tiled=False)
    right_panel = column_slab(masked)
    shift = row_index * tile_rows - col_index * tile_cols
    place = jnp.stack([shift, col_index, jnp.int32(order_total)]).astype(jnp.int32)
    squared, traces = panel_product(
        place, left_panel, right_panel, keep_mask.astype(jnp.int32)
    )
    for axis in reversed(ROW_COL):
        traces = lax.psum(traces, axis)
    return (squared, traces)


def solution(mesh):
    torus = Mesh(
        mesh.devices.reshape(12, 2, 4, 4, 2), ("row_0", "row_1", "col_0", "col_1", "col_2")
    )
    placed = (P(ROW, COL), P())
    return jax.shard_map(
        on_device, mesh=torus, in_specs=placed, out_specs=(P(ROW, COL), P()), check_vma=False
    )
```
